32 devices in a mesh: depth: 2 (over y), row: 4 (over x, core), col: 4 (over z).
Axes of the slice: x: 2, y: 2, z: 4, core: 2. Of those that a mesh axis runs over, the one named last changes fastest.
Arguments:
- tokens: bfloat16 [512, 16384], P('col', ('depth', 'row')), may hold values from -6 to 6
- weight: bfloat16 [16384, 26624], P(('depth', 'row'), 'col'), may hold values from -0.0625 to 0.0625
Outputs:
- hidden: bfloat16 [512, 4, 6656], P('row', 'col', 'depth')
The draws below stay inside these ranges and needn't reach their ends.
All inputs are finite; a program needn't handle non-finite values.
Results may differ from the reference program's by a relative error of at most 0.001.
Values may be sent and summed in bfloat16 or wider, within the bound.
No kernel may reach another device: no remote copies, remote signals or barrier semaphores. Data moves between devices by JAX's collectives and lax.ppermute only.
A program may use at most 128 MiB of HBM per device.

```python
import jax
import jax.numpy as jnp

D = 16384
FFW = 26624
TOKENS = 512
COLS = 6656
N_COL = 4


def strengthened(values, stream_key, source, target, shards_of, factor):
    owner, partner = [(jnp.arange(values.shape[axis_at]) // (values.shape[axis_at] // shards_of)).reshape([-1 if axis == axis_at else 1 for axis in range(values.ndim)]) for axis_at in (source, target)]
    chosen = jax.random.permutation(stream_key, shards_of)[partner]
    strong = (owner == chosen) | (owner == (partner + shards_of // 2) % shards_of)
    return jnp.where(strong, factor * values, values)


def level_of(own_key, shape, split, low, top_value):
    loudness = 1.0
    for axis_at, shards_of in split:
        draws = jax.random.uniform(jax.random.fold_in(jax.random.fold_in(own_key, 6), axis_at), (shards_of,), jnp.float32, low / len(split), top_value / len(split))
        loudness = loudness * jnp.repeat(jnp.exp(draws), shape[axis_at] // shards_of).reshape((-1,) + (1,) * (len(shape) - 1 - axis_at))
    return loudness


def bell_draw(stream_key, dims, width, reach, split=(), held_as=jnp.bfloat16):
    array = width * jax.random.normal(stream_key, dims, jnp.float32)
    if split:
        array = array * level_of(stream_key, dims, split, -0.22, 0.18)
    return jnp.clip(array, -reach, reach).astype(held_as)


def heavy_noise(key, dims, width, reach, cuts, heavy, held_as=jnp.bfloat16):
    result = width * jax.random.normal(key, dims, jnp.float32)
    if cuts:
        result = result * level_of(key, dims, cuts, -0.22, 0.18)
    return jnp.clip(strengthened(result, jax.random.fold_in(key, 3), *heavy), -reach, reach).astype(held_as)


def setup_inputs(seed: int = 0) -> dict:
    key_of = jax.random.split(jax.random.key(seed), 3)
    return {
        "tokens": bell_draw(key_of[0], (TOKENS, D), 1.0, 6.0, ((0, 4), (1, 8))),
        "weight": heavy_noise(key_of[1], (D, FFW), D ** -0.5, 0.0625, ((0, 8), (1, 4)), (0, 1, 8, 2.0)),
    }


def reference(tokens, weight):
    product = jnp.dot(tokens, weight, preferred_element_type=jnp.float32)
    return product.astype(jnp.bfloat16).reshape(TOKENS, N_COL, COLS)
```

```python
import jax
import jax.numpy as jnp
from jax import lax
from jax.sharding import PartitionSpec as P


def ring_reduce_scatter(x, dim, size, index, shift):
    if size == 1:
        return lax.index_in_dim(x, 0, dim, keepdims=False)
    buf = lax.dynamic_index_in_dim(x, (index - 1) % size, dim, keepdims=False)
    for step in range(size - 1):
        received = shift(buf)
        chunk = (index - step - 2) % size
        buf = received + lax.dynamic_index_in_dim(x, chunk, dim, keepdims=False)
    return buf


def local(tokens, weight):
    n_row = lax.axis_size("row")
    n_depth = lax.axis_size("depth")
    row = lax.axis_index("row")
    depth = lax.axis_index("depth")
    core = row % 2
    hi = row // 2
    n_hi = n_row // 2

    gathered = lax.all_gather(tokens, "col", axis=0, tiled=True)
    product = jnp.dot(gathered, weight, preferred_element_type=jnp.float32)
    total, width = product.shape
    block = total // n_row
    part = width // n_depth
    product = product.reshape(n_hi, 2, block, n_depth, part)

    keep = lax.dynamic_index_in_dim(product, core, 1, keepdims=False)
    send = lax.dynamic_index_in_dim(product, 1 - core, 1, keepdims=False)
    partner = [(q, q ^ 1) for q in range(n_row)]
    summed = keep + lax.ppermute(send, "row", partner)

    def shift_hi(value):
        pairs = [(h * 2 + c, ((h + 1) % n_hi) * 2 + c) for h in range(n_hi) for c in range(2)]
        return lax.ppermute(value, "row", pairs)

    def shift_depth(value):
        pairs = [(q, (q + 1) % n_depth) for q in range(n_depth)]
        return lax.ppermute(value, "depth", pairs)

    half = block // 2
    first = summed[:, :half]
    second = summed[:, half:]
    first = ring_reduce_scatter(first, 0, n_hi, hi, shift_hi)
    first = ring_reduce_scatter(first, 1, n_depth, depth, shift_depth)
    second = ring_reduce_scatter(second, 2, n_depth, depth, shift_depth)
    second = ring_reduce_scatter(second, 0, n_hi, hi, shift_hi)
    shares = jnp.concatenate([first, second], axis=0)
    return shares.astype(jnp.bfloat16).reshape(block, 1, part)


def solution(mesh):
    in_specs = (P("col", ("depth", "row")), P(("depth", "row"), "col"))
    out_specs = P("row", "col", "depth")
    return jax.shard_map(local, mesh=mesh, in_specs=in_specs, out_specs=out_specs, check_vma=False)
```

```python
import jax
import jax.numpy as jnp
from jax import lax
from jax.sharding import PartitionSpec as P


def ring_reduce_scatter(x, dim, size, index, shift):
    if size == 1:
        return lax.index_in_dim(x, 0, dim, keepdims=False)
    buf = lax.dynamic_index_in_dim(x, (index - 1) % size, dim, keepdims=False)
    for step in range(size - 1):
        received = shift(buf)
        chunk = (index - step - 2) % size
        buf = received + lax.dynamic_index_in_dim(x, chunk, dim, keepdims=False)
    return buf


def gather_tokens(tokens, n_col, col):
    received = [tokens]
    for steps in range(1, n_col):
        pairs = [(q, (q + steps) % n_col) for q in range(n_col)]
        received.append(lax.ppermute(tokens, "col", pairs))
    stacked = jnp.stack(received)
    order = (col - jnp.arange(n_col)) % n_col
    gathered = jnp.take(stacked, order, axis=0)
    return gathered.reshape(n_col * tokens.shape[0], tokens.shape[1])


def local(tokens, weight):
    n_row = lax.axis_size("row")
    n_depth = lax.axis_size("depth")
    n_col = lax.axis_size("col")
    row = lax.axis_index("row")
    depth = lax.axis_index("depth")
    col = lax.axis_index("col")
    core = row % 2
    hi = row // 2
    n_hi = n_row // 2

    gathered = gather_tokens(tokens, n_col, col)
    total = gathered.shape[0]
    width = weight.shape[1]
    block = total // n_row
    part = width // n_depth
    half = block // 2
    chunks = 2 if part % 256 == 0 else 1
    piece = part // chunks

    by_block = gathered.reshape(n_hi, 2, block, gathered.shape[1])
    own_rows = lax.dynamic_index_in_dim(by_block, core, 1, keepdims=False).reshape(n_hi * block, -1)
    other_rows = lax.dynamic_index_in_dim(by_block, 1 - core, 1, keepdims=False).reshape(n_hi * block, -1)

    partner = [(q, q ^ 1) for q in range(n_row)]

    def shift_hi(value):
        pairs = [(h * 2 + c, ((h + 1) % n_hi) * 2 + c) for h in range(n_hi) for c in range(2)]
        return lax.ppermute(value, "row", pairs)

    def shift_depth(value):
        pairs = [(q, (q + 1) % n_depth) for q in range(n_depth)]
        return lax.ppermute(value, "depth", pairs)

    def columns(d, q):
        start = d * part + q * piece
        return weight[:, start:start + piece]

    firsts, seconds = [], []
    for q in range(chunks):
        sent = [jnp.dot(other_rows, columns(d, q), preferred_element_type=jnp.float32) for d in range(n_depth)]
        arrived = lax.ppermute(sent, "row", partner)
        kept = [jnp.dot(own_rows, columns(d, q), preferred_element_type=jnp.float32) for d in range(n_depth)]
        summed = jnp.stack([(k + a).reshape(n_hi, block, piece) for k, a in zip(kept, arrived)])
        first = summed[:, :, :half]
        second = summed[:, :, half:]
        first = ring_reduce_scatter(first, 1, n_hi, hi, shift_hi)
        first = ring_reduce_scatter(first, 0, n_depth, depth, shift_depth)
        second = ring_reduce_scatter(second, 0, n_depth, depth, shift_depth)
        second = ring_reduce_scatter(second, 0, n_hi, hi, shift_hi)
        firsts.append(first)
        seconds.append(second)
    shares = jnp.concatenate(
        [jnp.concatenate(firsts, axis=1), jnp.concatenate(seconds, axis=1)], axis=0
    )
    return shares.astype(jnp.bfloat16).reshape(block, 1, part)


def solution(mesh):
    in_specs = (P("col", ("depth", "row")), P(("depth", "row"), "col"))
    out_specs = P("row", "col", "depth")
    return jax.shard_map(local, mesh=mesh, in_specs=in_specs, out_specs=out_specs, check_vma=False)
```

```python
import jax
import jax.numpy as jnp
from jax import lax
from jax.sharding import PartitionSpec as P


def ring_reduce_scatter(x, dim, size, index, shift):
    if size == 1:
        return lax.index_in_dim(x, 0, dim, keepdims=False)
    buf = lax.dynamic_index_in_dim(x, (index - 1) % size, dim, keepdims=False)
    for step in range(size - 1):
        received = shift(buf)
        chunk = (index - step - 2) % size
        buf = received + lax.dynamic_index_in_dim(x, chunk, dim, keepdims=False)
    return buf


def gather_tokens(tokens, n_col, col):
    rightward = [(q, q + 1) for q in range(n_col - 1)]
    leftward = [(q + 1, q) for q in range(n_col - 1)]
    from_left, from_right = [], []
    going_right = going_left = tokens
    for _ in range(1, n_col):
        going_right = lax.ppermute(going_right, "col", rightward)
        going_left = lax.ppermute(going_left, "col", leftward)
        from_left.append(going_right)
        from_right.append(going_left)
    line = jnp.stack(from_left[::-1] + [tokens] + from_right)
    gathered = lax.dynamic_slice_in_dim(line, n_col - 1 - col, n_col, 0)
    return gathered.reshape(n_col * tokens.shape[0], tokens.shape[1])


def local(tokens, weight):
    n_row = lax.axis_size("row")
    n_depth = lax.axis_size("depth")
    n_col = lax.axis_size("col")
    row = lax.axis_index("row")
    depth = lax.axis_index("depth")
    col = lax.axis_index("col")
    core = row % 2
    hi = row // 2
    n_hi = n_row // 2

    gathered = gather_tokens(tokens, n_col, col)
    total = gathered.shape[0]
    width = weight.shape[1]
    block = total // n_row
    part = width // n_depth
    half = block // 2
    lanes = part // 128 if part % 128 == 0 else 1
    chunks = min(4, lanes)
    bounds = [(lanes * q // chunks) * (part // lanes) for q in range(chunks + 1)]

    by_block = gathered.reshape(n_hi, 2, block, gathered.shape[1])
    own_rows = lax.dynamic_index_in_dim(by_block, core, 1, keepdims=False).reshape(n_hi * block, -1)
    other_rows = lax.dynamic_index_in_dim(by_block, 1 - core, 1, keepdims=False).reshape(n_hi * block, -1)

    partner = [(q, q ^ 1) for q in range(n_row)]

    def shift_hi(value):
        pairs = [(h * 2 + c, ((h + 1) % n_hi) * 2 + c) for h in range(n_hi) for c in range(2)]
        return lax.ppermute(value, "row", pairs)

    def shift_depth(value):
        pairs = [(q, (q + 1) % n_depth) for q in range(n_depth)]
        return lax.ppermute(value, "depth", pairs)

    def columns(d, q):
        return weight[:, d * part + bounds[q]:d * part + bounds[q + 1]]

    firsts, seconds = [], []
    for q in range(chunks):
        sent = [jnp.dot(other_rows, columns(d, q), preferred_element_type=jnp.float32) for d in range(n_depth)]
        arrived = lax.ppermute(sent, "row", partner)
        kept = [jnp.dot(own_rows, columns(d, q), preferred_element_type=jnp.float32) for d in range(n_depth)]
        summed = jnp.stack([(k + a).reshape(n_hi, block, -1) for k, a in zip(kept, arrived)])
        first = summed[:, :, :half]
        second = summed[:, :, half:]
        first = ring_reduce_scatter(first, 1, n_hi, hi, shift_hi)
        first = ring_reduce_scatter(first, 0, n_depth, depth, shift_depth)
        second = ring_reduce_scatter(second, 0, n_depth, depth, shift_depth)
        second = ring_reduce_scatter(second, 0, n_hi, hi, shift_hi)
        firsts.append(first)
        seconds.append(second)
    shares = jnp.concatenate(
        [jnp.concatenate(firsts, axis=1), jnp.concatenate(seconds, axis=1)], axis=0
    )
    return shares.astype(jnp.bfloat16).reshape(block, 1, part)


def solution(mesh):
    in_specs = (P("col", ("depth", "row")), P(("depth", "row"), "col"))
    out_specs = P("row", "col", "depth")
    return jax.shard_map(local, mesh=mesh, in_specs=in_specs, out_specs=out_specs, check_vma=False)
```

```python
import jax
import jax.numpy as jnp
from jax import lax
from jax.sharding import PartitionSpec as P


def ring_reduce_scatter(x, dim, size, index, shift):
    if size == 1:
        return lax.index_in_dim(x, 0, dim, keepdims=False)
    buf = lax.dynamic_index_in_dim(x, (index - 1) % size, dim, keepdims=False)
    for step in range(size - 1):
        received = shift(buf)
        chunk = (index - step - 2) % size
        buf = received + lax.dynamic_index_in_dim(x, chunk, dim, keepdims=False)
    return buf


def relay_tokens(tokens, n_col):
    rightward = [(q, q + 1) for q in range(n_col - 1)]
    leftward = [(q + 1, q) for q in range(n_col - 1)]
    from_left, from_right = [], []
    going_right = going_left = tokens
    for _ in range(1, n_col):
        going_right = lax.ppermute(going_right, "col", rightward)
        going_left = lax.ppermute(going_left, "col", leftward)
        from_left.append(going_right)
        from_right.append(going_left)
    return from_left, from_right


def gather_tokens(tokens, n_col, col):
    from_left, from_right = relay_tokens(tokens, n_col)
    line = jnp.stack(from_left[::-1] + [tokens] + from_right)
    gathered = lax.dynamic_slice_in_dim(line, n_col - 1 - col, n_col, 0)
    return gathered.reshape(n_col * tokens.shape[0], tokens.shape[1])


def local(tokens, weight):
    n_row = lax.axis_size("row")
    n_depth = lax.axis_size("depth")
    n_col = lax.axis_size("col")
    row = lax.axis_index("row")
    depth = lax.axis_index("depth")
    col = lax.axis_index("col")
    core = row % 2
    hi = row // 2
    n_hi = n_row // 2

    total = tokens.shape[0] * n_col
    width = weight.shape[1]
    block = total // n_row
    part = width // n_depth
    half = block // 2
    lanes = part // 128 if part % 128 == 0 else 1
    chunks = min(4, lanes)
    bounds = [(lanes * q // chunks) * (part // lanes) for q in range(chunks + 1)]

    partner = [(q, q ^ 1) for q in range(n_row)]

    def shift_hi(value):
        pairs = [(h * 2 + c, ((h + 1) % n_hi) * 2 + c) for h in range(n_hi) for c in range(2)]
        return lax.ppermute(value, "row", pairs)

    def shift_depth(value):
        pairs = [(q, (q + 1) % n_depth) for q in range(n_depth)]
        return lax.ppermute(value, "depth", pairs)

    def columns(d, q):
        return weight[:, d * part + bounds[q]:d * part + bounds[q + 1]]

    if n_row == 4 and n_col == 4 and block == tokens.shape[0]:
        from_left, from_right = relay_tokens(tokens, n_col)
        even = col % 2 == 0
        low = col < 2
        mine = col % 2 == core
        next_block = jnp.where(even, from_right[0], from_left[0])
        far_block = jnp.where(low, from_right[1], from_left[1])
        last_block = jnp.where(
            col == 0, from_right[2],
            jnp.where(col == 1, from_right[0], jnp.where(col == 2, from_left[0], from_left[2])),
        )

        def stage(kept_tokens, sent_tokens):
            both = jnp.concatenate([sent_tokens, kept_tokens])
            pieces = []
            for q in range(chunks):
                products = [jnp.dot(both, columns(d, q), preferred_element_type=jnp.float32) for d in range(n_depth)]
                arrived = lax.ppermute([p[:block] for p in products], "row", partner)
                summed = jnp.stack([p[block:] + a for p, a in zip(products, arrived)])
                pair = ring_reduce_scatter(summed, 0, n_depth, depth, shift_depth)
                pieces.append(pair + shift_hi(pair))
            return jnp.concatenate(pieces, axis=1)

        first = stage(jnp.where(mine, tokens, next_block), jnp.where(mine, next_block, tokens))
        second = stage(jnp.where(mine, far_block, last_block), jnp.where(mine, last_block, far_block))
        shares = jnp.where(hi == col // 2, first, second)
        return shares.astype(jnp.bfloat16).reshape(block, 1, part)

    gathered = gather_tokens(tokens, n_col, col)
    by_block = gathered.reshape(n_hi, 2, block, gathered.shape[1])
    own_rows = lax.dynamic_index_in_dim(by_block, core, 1, keepdims=False).reshape(n_hi * block, -1)
    other_rows = lax.dynamic_index_in_dim(by_block, 1 - core, 1, keepdims=False).reshape(n_hi * block, -1)

    firsts, seconds = [], []
    for q in range(chunks):
        sent = [jnp.dot(other_rows, columns(d, q), preferred_element_type=jnp.float32) for d in range(n_depth)]
        arrived = lax.ppermute(sent, "row", partner)
        kept = [jnp.dot(own_rows, columns(d, q), preferred_element_type=jnp.float32) for d in range(n_depth)]
        summed = jnp.stack([(k + a).reshape(n_hi, block, -1) for k, a in zip(kept, arrived)])
        first = summed[:, :, :half]
        second = summed[:, :, half:]
        first = ring_reduce_scatter(first, 1, n_hi, hi, shift_hi)
        first = ring_reduce_scatter(first, 0, n_depth, depth, shift_depth)
        second = ring_reduce_scatter(second, 0, n_depth, depth, shift_depth)
        second = ring_reduce_scatter(second, 0, n_hi, hi, shift_hi)
        firsts.append(first)
        seconds.append(second)
    shares = jnp.concatenate(
        [jnp.concatenate(firsts, axis=1), jnp.concatenate(seconds, axis=1)], axis=0
    )
    return shares.astype(jnp.bfloat16).reshape(block, 1, part)


def solution(mesh):
    in_specs = (P("col", ("depth", "row")), P(("depth", "row"), "col"))
    out_specs = P("row", "col", "depth")
    return jax.shard_map(local, mesh=mesh, in_specs=in_specs, out_specs=out_specs, check_vma=False)
```

```python
import jax
import jax.numpy as jnp
from jax import lax
from jax.sharding import PartitionSpec as P


def ring_reduce_scatter(x, dim, size, index, shift):
    if size == 1:
        return lax.index_in_dim(x, 0, dim, keepdims=False)
    buf = lax.dynamic_index_in_dim(x, (index - 1) % size, dim, keepdims=False)
    for step in range(size - 1):
        received = shift(buf)
        chunk = (index - step - 2) % size
        buf = received + lax.dynamic_index_in_dim(x, chunk, dim, keepdims=False)
    return buf


def relay_tokens(tokens, n_col):
    rightward = [(q, q + 1) for q in range(n_col - 1)]
    leftward = [(q + 1, q) for q in range(n_col - 1)]
    from_left, from_right = [], []
    going_right = going_left = tokens
    for _ in range(1, n_col):
        going_right = lax.ppermute(going_right, "col", rightward)
        going_left = lax.ppermute(going_left, "col", leftward)
        from_left.append(going_right)
        from_right.append(going_left)
    return from_left, from_right


def gather_tokens(tokens, n_col, col):
    from_left, from_right = relay_tokens(tokens, n_col)
    line = jnp.stack(from_left[::-1] + [tokens] + from_right)
    gathered = lax.dynamic_slice_in_dim(line, n_col - 1 - col, n_col, 0)
    return gathered.reshape(n_col * tokens.shape[0], tokens.shape[1])


def local(tokens, weight):
    n_row = lax.axis_size("row")
    n_depth = lax.axis_size("depth")
    n_col = lax.axis_size("col")
    row = lax.axis_index("row")
    depth = lax.axis_index("depth")
    col = lax.axis_index("col")
    core = row % 2
    hi = row // 2
    n_hi = n_row // 2

    total = tokens.shape[0] * n_col
    width = weight.shape[1]
    block = total // n_row
    part = width // n_depth
    half = block // 2
    lanes = part // 128 if part % 128 == 0 else 1
    chunks = min(4, lanes)
    bounds = [(lanes * q // chunks) * (part // lanes) for q in range(chunks + 1)]

    partner = [(q, q ^ 1) for q in range(n_row)]

    def shift_hi(value):
        pairs = [(h * 2 + c, ((h + 1) % n_hi) * 2 + c) for h in range(n_hi) for c in range(2)]
        return lax.ppermute(value, "row", pairs)

    def shift_depth(value):
        pairs = [(q, (q + 1) % n_depth) for q in range(n_depth)]
        return lax.ppermute(value, "depth", pairs)

    def columns(d, q):
        return weight[:, d * part + bounds[q]:d * part + bounds[q + 1]]

    if n_row == 4 and n_col == 4 and block == tokens.shape[0]:
        from_left, from_right = relay_tokens(tokens, n_col)
        even = col % 2 == 0
        low = col < 2
        mine = col % 2 == core
        next_block = jnp.where(even, from_right[0], from_left[0])
        first_kept = jnp.where(mine, tokens, next_block)
        first_sent = jnp.where(mine, next_block, tokens)
        first_kept, first_sent, tokens, near_left, near_right = lax.optimization_barrier(
            (first_kept, first_sent, tokens, from_left[0], from_right[0])
        )
        far_block = jnp.where(low, from_right[1], from_left[1])
        last_block = jnp.where(
            col == 0, from_right[2],
            jnp.where(col == 1, near_right, jnp.where(col == 2, near_left, from_left[2])),
        )

        def stage(kept_tokens, sent_tokens):
            both = jnp.concatenate([sent_tokens, kept_tokens])
            pieces = []
            for q in range(chunks):
                products = [jnp.dot(both, columns(d, q), preferred_element_type=jnp.float32) for d in range(n_depth)]
                arrived = lax.ppermute([p[:block] for p in products], "row", partner)
                summed = jnp.stack([p[block:] + a for p, a in zip(products, arrived)])
                pair = ring_reduce_scatter(summed, 0, n_depth, depth, shift_depth)
                pieces.append(pair + shift_hi(pair))
            return jnp.concatenate(pieces, axis=1)

        first = stage(first_kept, first_sent)
        second = stage(jnp.where(mine, far_block, last_block), jnp.where(mine, last_block, far_block))
        shares = jnp.where(hi == col // 2, first, second)
        return shares.astype(jnp.bfloat16).reshape(block, 1, part)

    gathered = gather_tokens(tokens, n_col, col)
    by_block = gathered.reshape(n_hi, 2, block, gathered.shape[1])
    own_rows = lax.dynamic_index_in_dim(by_block, core, 1, keepdims=False).reshape(n_hi * block, -1)
    other_rows = lax.dynamic_index_in_dim(by_block, 1 - core, 1, keepdims=False).reshape(n_hi * block, -1)

    firsts, seconds = [], []
    for q in range(chunks):
        sent = [jnp.dot(other_rows, columns(d, q), preferred_element_type=jnp.float32) for d in range(n_depth)]
        arrived = lax.ppermute(sent, "row", partner)
        kept = [jnp.dot(own_rows, columns(d, q), preferred_element_type=jnp.float32) for d in range(n_depth)]
        summed = jnp.stack([(k + a).reshape(n_hi, block, -1) for k, a in zip(kept, arrived)])
        first = summed[:, :, :half]
        second = summed[:, :, half:]
        first = ring_reduce_scatter(first, 1, n_hi, hi, shift_hi)
        first = ring_reduce_scatter(first, 0, n_depth, depth, shift_depth)
        second = ring_reduce_scatter(second, 0, n_depth, depth, shift_depth)
        second = ring_reduce_scatter(second, 0, n_hi, hi, shift_hi)
        firsts.append(first)
        seconds.append(second)
    shares = jnp.concatenate(
        [jnp.concatenate(firsts, axis=1), jnp.concatenate(seconds, axis=1)], axis=0
    )
    return shares.astype(jnp.bfloat16).reshape(block, 1, part)


def solution(mesh):
    in_specs = (P("col", ("depth", "row")), P(("depth", "row"), "col"))
    out_specs = P("row", "col", "depth")
    return jax.shard_map(local, mesh=mesh, in_specs=in_specs, out_specs=out_specs, check_vma=False)
```

```python
import jax
import jax.numpy as jnp
from jax import lax
from jax.sharding import PartitionSpec as P


def ring_reduce_scatter(x, dim, size, index, shift):
    if size == 1:
        return lax.index_in_dim(x, 0, dim, keepdims=False)
    buf = lax.dynamic_index_in_dim(x, (index - 1) % size, dim, keepdims=False)
    for step in range(size - 1):
        received = shift(buf)
        chunk = (index - step - 2) % size
        buf = received + lax.dynamic_index_in_dim(x, chunk, dim, keepdims=False)
    return buf


def gather_tokens(tokens, n_col, col):
    rightward = [(q, q + 1) for q in range(n_col - 1)]
    leftward = [(q + 1, q) for q in range(n_col - 1)]
    from_left, from_right = [], []
    going_right = going_left = tokens
    for _ in range(1, n_col):
        going_right = lax.ppermute(going_right, "col", rightward)
        going_left = lax.ppermute(going_left, "col", leftward)
        from_left.append(going_right)
        from_right.append(going_left)
    line = jnp.stack(from_left[::-1] + [tokens] + from_right)
    gathered = lax.dynamic_slice_in_dim(line, n_col - 1 - col, n_col, 0)
    return gathered.reshape(n_col * tokens.shape[0], tokens.shape[1])


def local(tokens, weight):
    n_row = lax.axis_size("row")
    n_depth = lax.axis_size("depth")
    n_col = lax.axis_size("col")
    row = lax.axis_index("row")
    depth = lax.axis_index("depth")
    col = lax.axis_index("col")
    core = row % 2
    hi = row // 2
    n_hi = n_row // 2

    gathered = gather_tokens(tokens, n_col, col)
    total = gathered.shape[0]
    width = weight.shape[1]
    block = total // n_row
    part = width // n_depth
    half = block // 2
    lanes = part // 128 if part % 128 == 0 else 1
    chunks = min(2, lanes)
    bounds = [(lanes * q // chunks) * (part // lanes) for q in range(chunks + 1)]

    by_block = gathered.reshape(n_hi, 2, block, gathered.shape[1])
    own_rows = lax.dynamic_index_in_dim(by_block, core, 1, keepdims=False).reshape(n_hi * block, -1)
    other_rows = lax.dynamic_index_in_dim(by_block, 1 - core, 1, keepdims=False).reshape(n_hi * block, -1)

    partner = [(q, q ^ 1) for q in range(n_row)]

    def shift_hi(value):
        pairs = [(h * 2 + c, ((h + 1) % n_hi) * 2 + c) for h in range(n_hi) for c in range(2)]
        return lax.ppermute(value, "row", pairs)

    def shift_depth(value):
        pairs = [(q, (q + 1) % n_depth) for q in range(n_depth)]
        return lax.ppermute(value, "depth", pairs)

    def columns(d, q):
        return weight[:, d * part + bounds[q]:d * part + bounds[q + 1]]

    firsts, seconds = [], []
    for q in range(chunks):
        sent = [jnp.dot(other_rows, columns(d, q), preferred_element_type=jnp.float32) for d in range(n_depth)]
        arrived = lax.ppermute(sent, "row", partner)
        kept = [jnp.dot(own_rows, columns(d, q), preferred_element_type=jnp.float32) for d in range(n_depth)]
        summed = jnp.stack([(k + a).reshape(n_hi, block, -1) for k, a in zip(kept, arrived)])
        first = summed[:, :, :half]
        second = summed[:, :, half:]
        first = ring_reduce_scatter(first, 1, n_hi, hi, shift_hi)
        first = ring_reduce_scatter(first, 0, n_depth, depth, shift_depth)
        second = ring_reduce_scatter(second, 0, n_depth, depth, shift_depth)
        second = ring_reduce_scatter(second, 0, n_hi, hi, shift_hi)
        firsts.append(first)
        seconds.append(second)
    shares = jnp.concatenate(
        [jnp.concatenate(firsts, axis=1), jnp.concatenate(seconds, axis=1)], axis=0
    )
    return shares.astype(jnp.bfloat16).reshape(block, 1, part)


def solution(mesh):
    in_specs = (P("col", ("depth", "row")), P(("depth", "row"), "col"))
    out_specs = P("row", "col", "depth")
    return jax.shard_map(local, mesh=mesh, in_specs=in_specs, out_specs=out_specs, check_vma=False)
```

```python
import jax
import jax.numpy as jnp
from jax import lax
from jax.sharding import PartitionSpec as P


def ring_reduce_scatter(x, dim, size, index, shift):
    if size == 1:
        return lax.index_in_dim(x, 0, dim, keepdims=False)
    buf = lax.dynamic_index_in_dim(x, (index - 1) % size, dim, keepdims=False)
    for step in range(size - 1):
        received = shift(buf)
        chunk = (index - step - 2) % size
        buf = received + lax.dynamic_index_in_dim(x, chunk, dim, keepdims=False)
    return buf


def gather_tokens(tokens, n_col, col):
    rightward = [(q, q + 1) for q in range(n_col - 1)]
    leftward = [(q + 1, q) for q in range(n_col - 1)]
    from_left, from_right = [], []
    going_right = going_left = tokens
    for _ in range(1, n_col):
        going_right = lax.ppermute(going_right, "col", rightward)
        going_left = lax.ppermute(going_left, "col", leftward)
        from_left.append(going_right)
        from_right.append(going_left)
    line = jnp.stack(from_left[::-1] + [tokens] + from_right)
    gathered = lax.dynamic_slice_in_dim(line, n_col - 1 - col, n_col, 0)
    return gathered.reshape(n_col * tokens.shape[0], tokens.shape[1])


def local(tokens, weight):
    n_row = lax.axis_size("row")
    n_depth = lax.axis_size("depth")
    n_col = lax.axis_size("col")
    row = lax.axis_index("row")
    depth = lax.axis_index("depth")
    col = lax.axis_index("col")
    core = row % 2
    hi = row // 2
    n_hi = n_row // 2

    gathered = gather_tokens(tokens, n_col, col)
    total = gathered.shape[0]
    width = weight.shape[1]
    block = total // n_row
    part = width // n_depth
    half = block // 2
    lanes = part // 128 if part % 128 == 0 else 1
    chunks = min(6, lanes)
    bounds = [(lanes * q // chunks) * (part // lanes) for q in range(chunks + 1)]

    by_block = gathered.reshape(n_hi, 2, block, gathered.shape[1])
    own_rows = lax.dynamic_index_in_dim(by_block, core, 1, keepdims=False).reshape(n_hi * block, -1)
    other_rows = lax.dynamic_index_in_dim(by_block, 1 - core, 1, keepdims=False).reshape(n_hi * block, -1)

    partner = [(q, q ^ 1) for q in range(n_row)]

    def shift_hi(value):
        pairs = [(h * 2 + c, ((h + 1) % n_hi) * 2 + c) for h in range(n_hi) for c in range(2)]
        return lax.ppermute(value, "row", pairs)

    def shift_depth(value):
        pairs = [(q, (q + 1) % n_depth) for q in range(n_depth)]
        return lax.ppermute(value, "depth", pairs)

    def columns(d, q):
        return weight[:, d * part + bounds[q]:d * part + bounds[q + 1]]

    firsts, seconds = [], []
    for q in range(chunks):
        sent = [jnp.dot(other_rows, columns(d, q), preferred_element_type=jnp.float32) for d in range(n_depth)]
        arrived = lax.ppermute(sent, "row", partner)
        kept = [jnp.dot(own_rows, columns(d, q), preferred_element_type=jnp.float32) for d in range(n_depth)]
        summed = jnp.stack([(k + a).reshape(n_hi, block, -1) for k, a in zip(kept, arrived)])
        first = summed[:, :, :half]
        second = summed[:, :, half:]
        first = ring_reduce_scatter(first, 1, n_hi, hi, shift_hi)
        first = ring_reduce_scatter(first, 0, n_depth, depth, shift_depth)
        second = ring_reduce_scatter(second, 0, n_depth, depth, shift_depth)
        second = ring_reduce_scatter(second, 0, n_hi, hi, shift_hi)
        firsts.append(first)
        seconds.append(second)
    shares = jnp.concatenate(
        [jnp.concatenate(firsts, axis=1), jnp.concatenate(seconds, axis=1)], axis=0
    )
    return shares.astype(jnp.bfloat16).reshape(block, 1, part)


def solution(mesh):
    in_specs = (P("col", ("depth", "row")), P(("depth", "row"), "col"))
    out_specs = P("row", "col", "depth")
    return jax.shard_map(local, mesh=mesh, in_specs=in_specs, out_specs=out_specs, check_vma=False)
```

```python
import jax
import jax.numpy as jnp
from jax import lax
from jax.sharding import PartitionSpec as P


def ring_reduce_scatter(x, dim, size, index, shift):
    if size == 1:
        return lax.index_in_dim(x, 0, dim, keepdims=False)
    buf = lax.dynamic_index_in_dim(x, (index - 1) % size, dim, keepdims=False)
    for step in range(size - 1):
        received = shift(buf)
        chunk = (index - step - 2) % size
        buf = received + lax.dynamic_index_in_dim(x, chunk, dim, keepdims=False)
    return buf


def gather_tokens(tokens, n_col, col):
    rightward = [(q, q + 1) for q in range(n_col - 1)]
    leftward = [(q + 1, q) for q in range(n_col - 1)]
    from_left, from_right = [], []
    going_right = going_left = tokens
    for _ in range(1, n_col):
        going_right = lax.ppermute(going_right, "col", rightward)
        going_left = lax.ppermute(going_left, "col", leftward)
        from_left.append(going_right)
        from_right.append(going_left)
    line = jnp.stack(from_left[::-1] + [tokens] + from_right)
    gathered = lax.dynamic_slice_in_dim(line, n_col - 1 - col, n_col, 0)
    return gathered.reshape(n_col * tokens.shape[0], tokens.shape[1])


def local(tokens, weight):
    n_row = lax.axis_size("row")
    n_depth = lax.axis_size("depth")
    n_col = lax.axis_size("col")
    row = lax.axis_index("row")
    depth = lax.axis_index("depth")
    col = lax.axis_index("col")
    core = row % 2
    hi = row // 2
    n_hi = n_row // 2

    split = (tokens.shape[1] // 2) // 128 * 128 if tokens.shape[1] >= 256 else 0
    if split:
        by_offload = lax.all_gather(tokens[:, :split], "col", axis=0, tiled=True)
        by_relay = gather_tokens(tokens[:, split:], n_col, col)
        gathered = jnp.concatenate([by_offload, by_relay], axis=1)
    else:
        gathered = gather_tokens(tokens, n_col, col)
    total = gathered.shape[0]
    width = weight.shape[1]
    block = total // n_row
    part = width // n_depth
    half = block // 2
    lanes = part // 128 if part % 128 == 0 else 1
    chunks = min(4, lanes)
    bounds = [(lanes * q // chunks) * (part // lanes) for q in range(chunks + 1)]

    by_block = gathered.reshape(n_hi, 2, block, gathered.shape[1])
    own_rows = lax.dynamic_index_in_dim(by_block, core, 1, keepdims=False).reshape(n_hi * block, -1)
    other_rows = lax.dynamic_index_in_dim(by_block, 1 - core, 1, keepdims=False).reshape(n_hi * block, -1)

    partner = [(q, q ^ 1) for q in range(n_row)]

    def shift_hi(value):
        pairs = [(h * 2 + c, ((h + 1) % n_hi) * 2 + c) for h in range(n_hi) for c in range(2)]
        return lax.ppermute(value, "row", pairs)

    def shift_depth(value):
        pairs = [(q, (q + 1) % n_depth) for q in range(n_depth)]
        return lax.ppermute(value, "depth", pairs)

    def columns(d, q):
        return weight[:, d * part + bounds[q]:d * part + bounds[q + 1]]

    firsts, seconds = [], []
    for q in range(chunks):
        sent = [jnp.dot(other_rows, columns(d, q), preferred_element_type=jnp.float32) for d in range(n_depth)]
        arrived = lax.ppermute(sent, "row", partner)
        kept = [jnp.dot(own_rows, columns(d, q), preferred_element_type=jnp.float32) for d in range(n_depth)]
        summed = jnp.stack([(k + a).reshape(n_hi, block, -1) for k, a in zip(kept, arrived)])
        first = summed[:, :, :half]
        second = summed[:, :, half:]
        first = ring_reduce_scatter(first, 1, n_hi, hi, shift_hi)
        first = ring_reduce_scatter(first, 0, n_depth, depth, shift_depth)
        second = ring_reduce_scatter(second, 0, n_depth, depth, shift_depth)
        second = ring_reduce_scatter(second, 0, n_hi, hi, shift_hi)
        firsts.append(first)
        seconds.append(second)
    shares = jnp.concatenate(
        [jnp.concatenate(firsts, axis=1), jnp.concatenate(seconds, axis=1)], axis=0
    )
    return shares.astype(jnp.bfloat16).reshape(block, 1, part)


def solution(mesh):
    in_specs = (P("col", ("depth", "row")), P(("depth", "row"), "col"))
    out_specs = P("row", "col", "depth")
    return jax.shard_map(local, mesh=mesh, in_specs=in_specs, out_specs=out_specs, check_vma=False)
```

```python
import jax
import jax.numpy as jnp
from jax import lax
from jax.sharding import PartitionSpec as P


def ring_reduce_scatter(x, dim, size, index, shift):
    if size == 1:
        return lax.index_in_dim(x, 0, dim, keepdims=False)
    buf = lax.dynamic_index_in_dim(x, (index - 1) % size, dim, keepdims=False)
    for step in range(size - 1):
        received = shift(buf)
        chunk = (index - step - 2) % size
        buf = received + lax.dynamic_index_in_dim(x, chunk, dim, keepdims=False)
    return buf


def gather_tokens(tokens, n_col, col):
    rightward = [(q, q + 1) for q in range(n_col - 1)]
    leftward = [(q + 1, q) for q in range(n_col - 1)]
    from_left, from_right = [], []
    going_right = going_left = tokens
    for _ in range(1, n_col):
        going_right = lax.ppermute(going_right, "col", rightward)
        going_left = lax.ppermute(going_left, "col", leftward)
        from_left.append(going_right)
        from_right.append(going_left)
    line = jnp.stack(from_left[::-1] + [tokens] + from_right)
    gathered = lax.dynamic_slice_in_dim(line, n_col - 1 - col, n_col, 0)
    return gathered.reshape(n_col * tokens.shape[0], tokens.shape[1])


def local(tokens, weight):
    n_row = lax.axis_size("row")
    n_depth = lax.axis_size("depth")
    n_col = lax.axis_size("col")
    row = lax.axis_index("row")
    depth = lax.axis_index("depth")
    col = lax.axis_index("col")
    core = row % 2
    hi = row // 2
    n_hi = n_row // 2

    gathered = gather_tokens(tokens, n_col, col)
    total = gathered.shape[0]
    width = weight.shape[1]
    block = total // n_row
    part = width // n_depth
    half = block // 2
    lanes = part // 128 if part % 128 == 0 else 1
    chunks = min(5, lanes)
    bounds = [(lanes * q // chunks) * (part // lanes) for q in range(chunks + 1)]

    by_block = gathered.reshape(n_hi, 2, block, gathered.shape[1])
    own_rows = lax.dynamic_index_in_dim(by_block, core, 1, keepdims=False).reshape(n_hi * block, -1)
    other_rows = lax.dynamic_index_in_dim(by_block, 1 - core, 1, keepdims=False).reshape(n_hi * block, -1)

    partner = [(q, q ^ 1) for q in range(n_row)]

    def shift_hi(value):
        pairs = [(h * 2 + c, ((h + 1) % n_hi) * 2 + c) for h in range(n_hi) for c in range(2)]
        return lax.ppermute(value, "row", pairs)

    def shift_depth(value):
        pairs = [(q, (q + 1) % n_depth) for q in range(n_depth)]
        return lax.ppermute(value, "depth", pairs)

    def columns(d, q):
        return weight[:, d * part + bounds[q]:d * part + bounds[q + 1]]

    firsts, seconds = [], []
    for q in range(chunks):
        sent = [jnp.dot(other_rows, columns(d, q), preferred_element_type=jnp.float32) for d in range(n_depth)]
        arrived = lax.ppermute(sent, "row", partner)
        kept = [jnp.dot(own_rows, columns(d, q), preferred_element_type=jnp.float32) for d in range(n_depth)]
        summed = jnp.stack([(k + a).reshape(n_hi, block, -1) for k, a in zip(kept, arrived)])
        first = summed[:, :, :half]
        second = summed[:, :, half:]
        first = ring_reduce_scatter(first, 1, n_hi, hi, shift_hi)
        first = ring_reduce_scatter(first, 0, n_depth, depth, shift_depth)
        second = ring_reduce_scatter(second, 0, n_depth, depth, shift_depth)
        second = ring_reduce_scatter(second, 0, n_hi, hi, shift_hi)
        firsts.append(first)
        seconds.append(second)
    shares = jnp.concatenate(
        [jnp.concatenate(firsts, axis=1), jnp.concatenate(seconds, axis=1)], axis=0
    )
    return shares.astype(jnp.bfloat16).reshape(block, 1, part)


def solution(mesh):
    in_specs = (P("col", ("depth", "row")), P(("depth", "row"), "col"))
    out_specs = P("row", "col", "depth")
    return jax.shard_map(local, mesh=mesh, in_specs=in_specs, out_specs=out_specs, check_vma=False)
```

```python
import jax
import jax.numpy as jnp
from jax import lax
from jax.sharding import PartitionSpec as P


def ring_reduce_scatter(x, dim, size, index, shift):
    if size == 1:
        return lax.index_in_dim(x, 0, dim, keepdims=False)
    buf = lax.dynamic_index_in_dim(x, (index - 1) % size, dim, keepdims=False)
    for step in range(size - 1):
        received = shift(buf)
        chunk = (index - step - 2) % size
        buf = received + lax.dynamic_index_in_dim(x, chunk, dim, keepdims=False)
    return buf


def gather_tokens(tokens, n_col, col):
    if n_col == 4:
        from_left = lax.ppermute(tokens, "col", [(0, 1), (1, 2), (2, 3)])
        from_right = lax.ppermute(tokens, "col", [(1, 0), (2, 1), (3, 2)])
        from_end = lax.ppermute(tokens, "col", [(0, 3), (3, 0)])
        two_left = lax.ppermute(from_left, "col", [(1, 2), (2, 3)])
        two_right = lax.ppermute(from_right, "col", [(2, 1), (1, 0)])
        line = jnp.stack([from_end, two_left, from_left, tokens, from_right, two_right, from_end])
        gathered = lax.dynamic_slice_in_dim(line, 3 - col, 4, 0)
        return gathered.reshape(4 * tokens.shape[0], tokens.shape[1])
    rightward = [(q, q + 1) for q in range(n_col - 1)]
    leftward = [(q + 1, q) for q in range(n_col - 1)]
    from_left, from_right = [], []
    going_right = going_left = tokens
    for _ in range(1, n_col):
        going_right = lax.ppermute(going_right, "col", rightward)
        going_left = lax.ppermute(going_left, "col", leftward)
        from_left.append(going_right)
        from_right.append(going_left)
    line = jnp.stack(from_left[::-1] + [tokens] + from_right)
    gathered = lax.dynamic_slice_in_dim(line, n_col - 1 - col, n_col, 0)
    return gathered.reshape(n_col * tokens.shape[0], tokens.shape[1])


def local(tokens, weight):
    n_row = lax.axis_size("row")
    n_depth = lax.axis_size("depth")
    n_col = lax.axis_size("col")
    row = lax.axis_index("row")
    depth = lax.axis_index("depth")
    col = lax.axis_index("col")
    core = row % 2
    hi = row // 2
    n_hi = n_row // 2

    gathered = gather_tokens(tokens, n_col, col)
    total = gathered.shape[0]
    width = weight.shape[1]
    block = total // n_row
    part = width // n_depth
    half = block // 2
    lanes = part // 128 if part % 128 == 0 else 1
    chunks = min(4, lanes)
    bounds = [(lanes * q // chunks) * (part // lanes) for q in range(chunks + 1)]

    by_block = gathered.reshape(n_hi, 2, block, gathered.shape[1])
    own_rows = lax.dynamic_index_in_dim(by_block, core, 1, keepdims=False).reshape(n_hi * block, -1)
    other_rows = lax.dynamic_index_in_dim(by_block, 1 - core, 1, keepdims=False).reshape(n_hi * block, -1)

    partner = [(q, q ^ 1) for q in range(n_row)]

    def shift_hi(value):
        pairs = [(h * 2 + c, ((h + 1) % n_hi) * 2 + c) for h in range(n_hi) for c in range(2)]
        return lax.ppermute(value, "row", pairs)

    def shift_depth(value):
        pairs = [(q, (q + 1) % n_depth) for q in range(n_depth)]
        return lax.ppermute(value, "depth", pairs)

    def columns(d, q):
        return weight[:, d * part + bounds[q]:d * part + bounds[q + 1]]

    firsts, seconds = [], []
    for q in range(chunks):
        sent = [jnp.dot(other_rows, columns(d, q), preferred_element_type=jnp.float32) for d in range(n_depth)]
        arrived = lax.ppermute(sent, "row", partner)
        kept = [jnp.dot(own_rows, columns(d, q), preferred_element_type=jnp.float32) for d in range(n_depth)]
        summed = jnp.stack([(k + a).reshape(n_hi, block, -1) for k, a in zip(kept, arrived)])
        first = summed[:, :, :half]
        second = summed[:, :, half:]
        first = ring_reduce_scatter(first, 1, n_hi, hi, shift_hi)
        first = ring_reduce_scatter(first, 0, n_depth, depth, shift_depth)
        second = ring_reduce_scatter(second, 0, n_depth, depth, shift_depth)
        second = ring_reduce_scatter(second, 0, n_hi, hi, shift_hi)
        firsts.append(first)
        seconds.append(second)
    shares = jnp.concatenate(
        [jnp.concatenate(firsts, axis=1), jnp.concatenate(seconds, axis=1)], axis=0
    )
    return shares.astype(jnp.bfloat16).reshape(block, 1, part)


def solution(mesh):
    in_specs = (P("col", ("depth", "row")), P(("depth", "row"), "col"))
    out_specs = P("row", "col", "depth")
    return jax.shard_map(local, mesh=mesh, in_specs=in_specs, out_specs=out_specs, check_vma=False)
```

```python
import jax
import jax.numpy as jnp
from jax import lax
from jax.sharding import PartitionSpec as P


def ring_reduce_scatter(x, dim, size, index, shift):
    if size == 1:
        return lax.index_in_dim(x, 0, dim, keepdims=False)
    buf = lax.dynamic_index_in_dim(x, (index - 1) % size, dim, keepdims=False)
    for step in range(size - 1):
        received = shift(buf)
        chunk = (index - step - 2) % size
        buf = received + lax.dynamic_index_in_dim(x, chunk, dim, keepdims=False)
    return buf


def gather_tokens(tokens, n_col, col):
    if n_col == 4:
        from_left = lax.ppermute(tokens, "col", [(0, 1), (1, 2), (2, 3)])
        from_right = lax.ppermute(tokens, "col", [(1, 0), (2, 1), (3, 2)])
        from_end = lax.ppermute(tokens, "col", [(0, 3), (3, 0)])
        two_left = lax.ppermute(from_left, "col", [(1, 2), (2, 3)])
        two_right = lax.ppermute(from_right, "col", [(2, 1), (1, 0)])
        line = jnp.stack([from_end, two_left, from_left, tokens, from_right, two_right, from_end])
        gathered = lax.dynamic_slice_in_dim(line, 3 - col, 4, 0)
        return gathered.reshape(4 * tokens.shape[0], tokens.shape[1])
    rightward = [(q, q + 1) for q in range(n_col - 1)]
    leftward = [(q + 1, q) for q in range(n_col - 1)]
    from_left, from_right = [], []
    going_right = going_left = tokens
    for _ in range(1, n_col):
        going_right = lax.ppermute(going_right, "col", rightward)
        going_left = lax.ppermute(going_left, "col", leftward)
        from_left.append(going_right)
        from_right.append(going_left)
    line = jnp.stack(from_left[::-1] + [tokens] + from_right)
    gathered = lax.dynamic_slice_in_dim(line, n_col - 1 - col, n_col, 0)
    return gathered.reshape(n_col * tokens.shape[0], tokens.shape[1])


def local(tokens, weight):
    n_row = lax.axis_size("row")
    n_depth = lax.axis_size("depth")
    n_col = lax.axis_size("col")
    row = lax.axis_index("row")
    depth = lax.axis_index("depth")
    col = lax.axis_index("col")
    core = row % 2
    hi = row // 2
    n_hi = n_row // 2

    gathered = gather_tokens(tokens, n_col, col)
    total = gathered.shape[0]
    width = weight.shape[1]
    block = total // n_row
    part = width // n_depth
    half = block // 2
    lanes = part // 128 if part % 128 == 0 else 1
    chunks = min(3, lanes)
    bounds = [(lanes * q // chunks) * (part // lanes) for q in range(chunks + 1)]

    by_block = gathered.reshape(n_hi, 2, block, gathered.shape[1])
    own_rows = lax.dynamic_index_in_dim(by_block, core, 1, keepdims=False).reshape(n_hi * block, -1)
    other_rows = lax.dynamic_index_in_dim(by_block, 1 - core, 1, keepdims=False).reshape(n_hi * block, -1)

    partner = [(q, q ^ 1) for q in range(n_row)]

    def shift_hi(value):
        pairs = [(h * 2 + c, ((h + 1) % n_hi) * 2 + c) for h in range(n_hi) for c in range(2)]
        return lax.ppermute(value, "row", pairs)

    def shift_depth(value):
        pairs = [(q, (q + 1) % n_depth) for q in range(n_depth)]
        return lax.ppermute(value, "depth", pairs)

    def columns(d, q):
        return weight[:, d * part + bounds[q]:d * part + bounds[q + 1]]

    firsts, seconds = [], []
    for q in range(chunks):
        sent = [jnp.dot(other_rows, columns(d, q), preferred_element_type=jnp.float32) for d in range(n_depth)]
        arrived = lax.ppermute(sent, "row", partner)
        kept = [jnp.dot(own_rows, columns(d, q), preferred_element_type=jnp.float32) for d in range(n_depth)]
        summed = jnp.stack([(k + a).reshape(n_hi, block, -1) for k, a in zip(kept, arrived)])
        first = summed[:, :, :half]
        second = summed[:, :, half:]
        first = ring_reduce_scatter(first, 1, n_hi, hi, shift_hi)
        first = ring_reduce_scatter(first, 0, n_depth, depth, shift_depth)
        second = ring_reduce_scatter(second, 0, n_depth, depth, shift_depth)
        second = ring_reduce_scatter(second, 0, n_hi, hi, shift_hi)
        firsts.append(first)
        seconds.append(second)
    shares = jnp.concatenate(
        [jnp.concatenate(firsts, axis=1), jnp.concatenate(seconds, axis=1)], axis=0
    )
    return shares.astype(jnp.bfloat16).reshape(block, 1, part)


def solution(mesh):
    in_specs = (P("col", ("depth", "row")), P(("depth", "row"), "col"))
    out_specs = P("row", "col", "depth")
    return jax.shard_map(local, mesh=mesh, in_specs=in_specs, out_specs=out_specs, check_vma=False)
```

```python
import jax
import jax.numpy as jnp
from jax import lax
from jax.sharding import PartitionSpec as P


def ring_reduce_scatter(x, dim, size, index, shift):
    if size == 1:
        return lax.index_in_dim(x, 0, dim, keepdims=False)
    buf = lax.dynamic_index_in_dim(x, (index - 1) % size, dim, keepdims=False)
    for step in range(size - 1):
        received = shift(buf)
        chunk = (index - step - 2) % size
        buf = received + lax.dynamic_index_in_dim(x, chunk, dim, keepdims=False)
    return buf


def gather_tokens(tokens, n_col, col):
    if n_col == 4:
        from_left = lax.ppermute(tokens, "col", [(0, 1), (1, 2), (2, 3)])
        from_right = lax.ppermute(tokens, "col", [(1, 0), (2, 1), (3, 2)])
        from_end = lax.ppermute(tokens, "col", [(0, 3), (3, 0)])
        two_left = lax.ppermute(from_left, "col", [(1, 2), (2, 3)])
        two_right = lax.ppermute(from_right, "col", [(2, 1), (1, 0)])
        line = jnp.stack([from_end, two_left, from_left, tokens, from_right, two_right, from_end])
        gathered = lax.dynamic_slice_in_dim(line, 3 - col, 4, 0)
        return gathered.reshape(4 * tokens.shape[0], tokens.shape[1])
    rightward = [(q, q + 1) for q in range(n_col - 1)]
    leftward = [(q + 1, q) for q in range(n_col - 1)]
    from_left, from_right = [], []
    going_right = going_left = tokens
    for _ in range(1, n_col):
        going_right = lax.ppermute(going_right, "col", rightward)
        going_left = lax.ppermute(going_left, "col", leftward)
        from_left.append(going_right)
        from_right.append(going_left)
    line = jnp.stack(from_left[::-1] + [tokens] + from_right)
    gathered = lax.dynamic_slice_in_dim(line, n_col - 1 - col, n_col, 0)
    return gathered.reshape(n_col * tokens.shape[0], tokens.shape[1])


def local(tokens, weight):
    n_row = lax.axis_size("row")
    n_depth = lax.axis_size("depth")
    n_col = lax.axis_size("col")
    row = lax.axis_index("row")
    depth = lax.axis_index("depth")
    col = lax.axis_index("col")
    core = row % 2
    hi = row // 2
    n_hi = n_row // 2

    gathered = gather_tokens(tokens, n_col, col)
    total = gathered.shape[0]
    width = weight.shape[1]
    block = total // n_row
    part = width // n_depth
    half = block // 2
    lanes = part // 128 if part % 128 == 0 else 1
    chunks = min(4, lanes)
    size = -(-lanes // chunks)
    first_size = lanes - size * (chunks - 1)
    if first_size > 0:
        bounds = [0] + [(first_size + size * q) * (part // lanes) for q in range(chunks)]
    else:
        bounds = [(lanes * q // chunks) * (part // lanes) for q in range(chunks + 1)]

    by_block = gathered.reshape(n_hi, 2, block, gathered.shape[1])
    own_rows = lax.dynamic_index_in_dim(by_block, core, 1, keepdims=False).reshape(n_hi * block, -1)
    other_rows = lax.dynamic_index_in_dim(by_block, 1 - core, 1, keepdims=False).reshape(n_hi * block, -1)

    partner = [(q, q ^ 1) for q in range(n_row)]

    def shift_hi(value):
        pairs = [(h * 2 + c, ((h + 1) % n_hi) * 2 + c) for h in range(n_hi) for c in range(2)]
        return lax.ppermute(value, "row", pairs)

    def shift_depth(value):
        pairs = [(q, (q + 1) % n_depth) for q in range(n_depth)]
        return lax.ppermute(value, "depth", pairs)

    def columns(d, q):
        return weight[:, d * part + bounds[q]:d * part + bounds[q + 1]]

    firsts, seconds = [], []
    for q in range(chunks):
        sent = [jnp.dot(other_rows, columns(d, q), preferred_element_type=jnp.float32) for d in range(n_depth)]
        arrived = lax.ppermute(sent, "row", partner)
        kept = [jnp.dot(own_rows, columns(d, q), preferred_element_type=jnp.float32) for d in range(n_depth)]
        summed = jnp.stack([(k + a).reshape(n_hi, block, -1) for k, a in zip(kept, arrived)])
        first = summed[:, :, :half]
        second = summed[:, :, half:]
        first = ring_reduce_scatter(first, 1, n_hi, hi, shift_hi)
        second = ring_reduce_scatter(second, 0, n_depth, depth, shift_depth)
        first = ring_reduce_scatter(first, 0, n_depth, depth, shift_depth)
        second = ring_reduce_scatter(second, 0, n_hi, hi, shift_hi)
        firsts.append(first)
        seconds.append(second)
    shares = jnp.concatenate(
        [jnp.concatenate(firsts, axis=1), jnp.concatenate(seconds, axis=1)], axis=0
    )
    return shares.astype(jnp.bfloat16).reshape(block, 1, part)


def solution(mesh):
    in_specs = (P("col", ("depth", "row")), P(("depth", "row"), "col"))
    out_specs = P("row", "col", "depth")
    return jax.shard_map(local, mesh=mesh, in_specs=in_specs, out_specs=out_specs, check_vma=False)
```
